768 devices in a mesh: shard: 48 (over z, x), cache: 16 (over y, core).
Axes of the slice: x: 4, y: 8, z: 12, core: 2. Of those that a mesh axis runs over, the one named last changes fastest.
Arguments:
- table: bfloat16 [786432, 256], P(('shard', 'cache'))
- panel_ids: int32 [2304], P(('shard', 'cache')), may hold values from 0 to 7, as said below
- bag_slots: int32 [16, 196608, 16], P('cache', 'shard'), may hold values from 0 to 2047
- block_ids: int32 [16, 1536, 16], P('cache', 'shard'), may hold values from 0 to 55
- bag_counts: int32 [16, 1536], P('cache', 'shard'), may hold values from 1 to 16, as said below
- dense_owner: int32 [768], P('shard'), may hold values from 0 to 15, as said below
- top_weight: bfloat16 [256, 1024], replicated, may hold values from -0.375 to 0.375
- bn_gain: float32 [1024], replicated, may hold values from 0.1 to 1.9
- bn_shift: float32 [1024], replicated, may hold values from -3 to 3
- out_weight: bfloat16 [1024], replicated, may hold values from -0.1875 to 0.1875
Outputs:
- top_hidden: bfloat16 [196608, 1024], P(('shard', 'cache'))
- logits: float32 [196608], P(('shard', 'cache'))
The draws below stay inside these ranges and needn't reach their ends.
Inputs may be any that keep to these rules, and one draw needn't show every extreme that they name: `bag_slots`: an entry v names row v % 128 of the block in place v // 128 of its bag block's list; places at or beyond the list's count are unused. `block_ids`: values below 48 name hot blocks of the group, the others own blocks of the feature's device. `bag_counts`: some bag block uses all 16 places. `panel_ids`: distinct within a device. `dense_owner`: each group of 16 consecutive entries is a permutation.
All inputs are finite; a program needn't handle non-finite values.
Results may differ from the reference program's by a relative error of at most 0.0055.
Values may be sent and summed in bfloat16 or wider, within the bound.
No kernel may reach another device: no remote copies, remote signals or barrier semaphores. Data moves between devices by JAX's collectives and lax.ppermute only.
A program may use at most 128 MiB of HBM per device.

```python
import jax
import jax.numpy as jnp
from jax import lax

E = 256
HID = 1024
F_DEV = 1
SAMP_DEV = 256
TAB_DEV = 1024
HOT_DEV = 3
L = 16
KMAX = 16
FEATS = 16
GROUP_SAMP = 4096
SAMPLES = 196608
ROWS = 786432
PANEL_BLOCKS = 48
SOURCE_BLOCKS = 56
HOT_TOTAL = 2304
BAG_BLOCKS = 1536
OWNER_SPANS = 768
N_CACHE = 16


def draw_table(key, part):
    shard_rows = TAB_DEV * (FEATS // F_DEV)
    shard_count = ROWS // shard_rows
    position = (jnp.arange(ROWS) // shard_rows).astype(jnp.float32) / max(shard_count - 1, 1)
    values = jax.random.normal(key, (ROWS, E), jnp.float32)
    scale = 0.2 * jnp.power(10.0, 0.5 * position)
    return (values * scale[:, None]).astype(jnp.bfloat16)


def draw_panel_ids(key, part):
    device_count = HOT_TOTAL // HOT_DEV
    key_list = jax.random.split(key, device_count)
    chosen = jax.vmap(lambda device_key: jax.random.permutation(device_key, TAB_DEV // 128)[:HOT_DEV])(key_list)
    return chosen.reshape(-1).astype(jnp.int32)


def draw_bag_counts(key, part):
    cache_devices = FEATS // F_DEV
    shard_groups = SAMPLES // GROUP_SAMP
    level_key, count_key, peak_key = jax.random.split(key, 3)
    levels = jax.random.randint(level_key, (cache_devices, shard_groups), 0, 4)
    ceilings = jnp.array([KMAX // 8, KMAX // 4, KMAX // 2, KMAX], jnp.int32)[levels]
    ceilings = jnp.repeat(jnp.repeat(ceilings, F_DEV, axis=0), GROUP_SAMP // 128, axis=1)
    counts = jax.random.randint(count_key, (FEATS, BAG_BLOCKS), 0, 1 << 20) % ceilings + 1
    peak = jax.random.randint(peak_key, (), 0, FEATS * BAG_BLOCKS)
    flat_counts = jnp.where(jnp.arange(FEATS * BAG_BLOCKS) == peak, KMAX, counts.reshape(-1))
    return flat_counts.reshape(FEATS, BAG_BLOCKS).astype(jnp.int32)


def draw_dense_owner(key, part):
    per_group = GROUP_SAMP // SAMP_DEV
    key_list = jax.random.split(key, OWNER_SPANS // per_group)
    chosen = jax.vmap(lambda group_key: jax.random.permutation(group_key, per_group))(key_list)
    return chosen.reshape(-1).astype(jnp.int32)


def set_ends(entries, own_key, smallest, high):
    longest = entries.shape.index(max(entries.shape))
    spots = []
    for shift in (0, 1):
        where = [jax.random.randint(jax.random.fold_in(own_key, axis), (), 0, length) for axis, length in enumerate(entries.shape)]
        where[longest] = (where[longest] + shift) % entries.shape[longest]
        spots.append(tuple(where))
    return entries.at[spots[0]].set(smallest).at[spots[1]].set(high)


def noise(rng, dims, width, limit, kind=jnp.bfloat16):
    entries = width * jax.random.normal(rng, dims, jnp.float32)
    return jnp.clip(entries, min=-limit, max=limit).astype(kind)


def setup_inputs(seed: int = 0) -> dict:
    splits = jax.random.split(jax.random.key(seed), 11)
    table = draw_table(jax.random.fold_in(splits[10], 71), 0)
    panel_ids = draw_panel_ids(jax.random.fold_in(splits[10], 71), 0)
    bag_slots = set_ends(jax.random.randint(splits[2], (FEATS, SAMPLES, L), 0, KMAX * 128), jax.random.fold_in(splits[2], 1), 0, (KMAX * 128) - 1).astype(jnp.int32)
    block_ids = set_ends(jax.random.randint(splits[3], (FEATS, BAG_BLOCKS, KMAX), 0, SOURCE_BLOCKS), jax.random.fold_in(splits[3], 1), 0, SOURCE_BLOCKS - 1).astype(jnp.int32)
    bag_counts = draw_bag_counts(jax.random.fold_in(splits[10], 71), 0)
    dense_owner = draw_dense_owner(jax.random.fold_in(splits[10], 71), 0)
    top_weight = noise(splits[6], (FEATS * FEATS, HID), (FEATS * FEATS) ** -0.5, 0.375)
    bn_gain = jnp.clip(1.0 + 0.18 * jax.random.normal(splits[7], (HID,), jnp.float32), 0.1, 1.9)
    bn_shift = noise(splits[8], (HID,), 0.5, 3.0, jnp.float32)
    out_weight = noise(splits[9], (HID,), HID ** -0.5, 0.1875)
    return {"table": table, "panel_ids": panel_ids, "bag_slots": bag_slots, "block_ids": block_ids, "bag_counts": bag_counts, "dense_owner": dense_owner, "top_weight": top_weight, "bn_gain": bn_gain, "bn_shift": bn_shift, "out_weight": out_weight}


norm_eps = 1e-05

def reference(table, panel_ids, bag_slots, block_ids, bag_counts, dense_owner, top_weight, bn_gain, bn_shift, out_weight):
    group_count = SAMPLES // GROUP_SAMP
    table_blocks = TAB_DEV // 128
    group_blocks = GROUP_SAMP // 128
    zero_index = jnp.zeros((), jnp.int32)

    def group_rows(group_id):
        group_id = group_id.astype(jnp.int32)
        device_rows = lax.dynamic_slice_in_dim(table, (group_id * (N_CACHE * TAB_DEV)).astype(jnp.int32), N_CACHE * TAB_DEV, 0)
        device_rows = device_rows.reshape(N_CACHE, table_blocks, 128, E)
        hot_picks = lax.dynamic_slice_in_dim(panel_ids, (group_id * (N_CACHE * HOT_DEV)).astype(jnp.int32), N_CACHE * HOT_DEV, 0)
        hot_picks = hot_picks.reshape(N_CACHE, HOT_DEV)
        hot_rows = jnp.take_along_axis(device_rows, hot_picks[:, :, None, None], axis=1).reshape(PANEL_BLOCKS * 128, E)

        def feature_rows(feature):
            feature = feature.astype(jnp.int32)
            own_index = (feature // F_DEV).astype(jnp.int32)
            own_rows = lax.dynamic_slice(device_rows, (own_index, zero_index, zero_index, zero_index), (1, table_blocks, 128, E))[0].reshape(TAB_DEV, E)
            source = jnp.concatenate([hot_rows, own_rows], axis=0)
            sample_start = (group_id * GROUP_SAMP).astype(jnp.int32)
            block_start = (group_id * group_blocks).astype(jnp.int32)
            slot_values = lax.dynamic_slice(bag_slots, (feature, sample_start, zero_index), (1, GROUP_SAMP, L))[0]
            list_ids = lax.dynamic_slice(block_ids, (feature, block_start, zero_index), (1, group_blocks, KMAX))[0]
            counts = lax.dynamic_slice(bag_counts, (feature, block_start), (1, group_blocks))[0]
            bag_block = (jnp.arange(GROUP_SAMP, dtype=jnp.int32) // 128)[:, None]
            list_slot = slot_values // 128
            in_list = list_slot < counts[bag_block]
            row_index = list_ids[bag_block, list_slot] * 128 + slot_values % 128
            picked = jnp.where(in_list[:, :, None], source[row_index].astype(jnp.float32), jnp.float32(0.0))
            return lax.optimization_barrier(jnp.sum(picked, axis=1)).astype(jnp.bfloat16)
        pooled = lax.map(feature_rows, jnp.arange(FEATS, dtype=jnp.int32))
        owners = lax.dynamic_slice_in_dim(dense_owner, (group_id * N_CACHE).astype(jnp.int32), N_CACHE, 0)
        owner_match = owners[None, :] == jnp.arange(N_CACHE, dtype=jnp.int32)[:, None]
        inverse = lax.optimization_barrier(jnp.sum(jnp.where(owner_match, jnp.arange(N_CACHE, dtype=jnp.int32)[None, :], 0), axis=1)).astype(jnp.int32)
        ordered = jnp.take(pooled.reshape(FEATS, N_CACHE, SAMP_DEV, E), inverse, axis=1)
        features = ordered.reshape(FEATS, GROUP_SAMP, E).astype(jnp.float32)
        products = jnp.einsum('fne,gne->nfg', features, features)
        interaction = (products / E ** 0.5).astype(jnp.bfloat16).reshape(GROUP_SAMP, FEATS * FEATS)
        return jnp.dot(interaction, top_weight, preferred_element_type=jnp.float32)
    pre_norm = lax.map(group_rows, jnp.arange(group_count, dtype=jnp.int32)).reshape(SAMPLES, HID)
    col_mean = lax.optimization_barrier(jnp.mean(pre_norm, axis=0))
    centered = pre_norm - col_mean
    col_var = lax.optimization_barrier(jnp.mean(centered * centered, axis=0))
    normed = centered * lax.rsqrt(col_var + norm_eps) * bn_gain + bn_shift
    top_hidden = jax.nn.relu(normed).astype(jnp.bfloat16)
    logits = jnp.dot(top_hidden, out_weight, preferred_element_type=jnp.float32)
    return (top_hidden, logits)
```

```python
import functools
import math

import jax
import jax.numpy as jnp
from jax import lax
from jax.experimental import pallas as pl
from jax.experimental.pallas import tpu as pltpu
from jax.sharding import PartitionSpec as P

norm_eps = 1e-05


def pool_kernel(order_ref, ids_ref, counts_ref, slots_ref, hot_ref, own_ref, out_ref, acc_ref):
    step = pl.program_id(0)
    block = order_ref[step]
    list_len = slots_ref.shape[1]
    hot_count = hot_ref.shape[0] // 128
    own_count = own_ref.shape[0] // 128
    slots = slots_ref[0]
    row_iota = lax.broadcasted_iota(jnp.int32, (128, 128), 0)
    acc_ref[...] = jnp.zeros(acc_ref.shape, jnp.float32)

    def place(k, carry):
        shifted = slots - k * 128
        hits = jnp.zeros((128, 128), jnp.float32)
        for entry in range(list_len):
            hits = hits + (shifted[entry : entry + 1, :] == row_iota).astype(jnp.float32)
        name = jnp.clip(ids_ref[block * list_len + k], 0, hot_count + own_count - 1)
        hot_start = pl.multiple_of(jnp.minimum(name, hot_count - 1) * 128, 128)
        own_start = pl.multiple_of(jnp.maximum(name - hot_count, 0) * 128, 128)
        rows = jnp.where(
            name < hot_count,
            hot_ref[pl.ds(hot_start, 128), :],
            own_ref[pl.ds(own_start, 128), :],
        )
        acc_ref[...] += lax.dot_general(
            hits.astype(jnp.bfloat16),
            rows,
            (((0,), (0,)), ((), ())),
            preferred_element_type=jnp.float32,
        )
        return carry

    count = jnp.clip(counts_ref[block], 0, list_len)
    lax.fori_loop(0, count, place, 0)
    out_ref[...] = acc_ref[...].astype(out_ref.dtype)


def pool(order, ids, counts, slots_t, hot, own):
    blocks, bag_len, _ = slots_t.shape
    width = hot.shape[1]
    grid_spec = pltpu.PrefetchScalarGridSpec(
        num_scalar_prefetch=3,
        grid=(blocks,),
        in_specs=[
            pl.BlockSpec((1, bag_len, 128), lambda i, o, d, c: (o[i], 0, 0)),
            pl.BlockSpec(hot.shape, lambda i, o, d, c: (0, 0)),
            pl.BlockSpec(own.shape, lambda i, o, d, c: (0, 0)),
        ],
        out_specs=pl.BlockSpec((128, width), lambda i, o, d, c: (i, 0)),
        scratch_shapes=[pltpu.VMEM((128, width), jnp.float32)],
    )
    return pl.pallas_call(
        pool_kernel,
        grid_spec=grid_spec,
        out_shape=jax.ShapeDtypeStruct((blocks * 128, width), jnp.bfloat16),
        compiler_params=pltpu.CompilerParams(
            dimension_semantics=("arbitrary",), vmem_limit_bytes=40 * 1024 * 1024
        ),
    )(order, ids, counts, slots_t, hot, own)


def shards(
    table,
    panel_ids,
    bag_slots,
    block_ids,
    bag_counts,
    dense_owner,
    top_weight,
    bn_gain,
    bn_shift,
    out_weight,
):
    row_width = table.shape[1]
    caches = lax.axis_size("cache")
    feat_dev, group_samp, bag_len = bag_slots.shape
    samp_dev = group_samp // caches
    owner_blocks = samp_dev // 128
    group_blocks = group_samp // 128
    blocks_dev = feat_dev * group_blocks
    list_len = block_ids.shape[2]
    hot_rows = jnp.take(table.reshape(-1, 128, row_width), panel_ids, axis=0).reshape(-1, row_width)
    cache_ids = jnp.arange(caches, dtype=jnp.int32)
    owner_match = dense_owner[None, :] == cache_ids[:, None]
    inverse = jnp.sum(jnp.where(owner_match, cache_ids[None, :], 0), axis=1)
    block_number = jnp.arange(blocks_dev, dtype=jnp.int32)
    feature_part = block_number // group_blocks
    within_group = block_number % group_blocks
    source_block = (
        feature_part * group_blocks
        + inverse[within_group // owner_blocks] * owner_blocks
        + within_group % owner_blocks
    ).astype(jnp.int32)
    slots_t = jnp.swapaxes(bag_slots.reshape(blocks_dev, 128, bag_len), 1, 2)
    ids = block_ids.reshape(blocks_dev * list_len).astype(jnp.int32)
    counts = bag_counts.reshape(blocks_dev).astype(jnp.int32)
    gathered = lax.all_gather(hot_rows, "cache", axis=0, tiled=True)
    pooled = pool(source_block, ids, counts, slots_t, gathered, table)
    pooled = pooled.reshape(feat_dev, caches, samp_dev, row_width)
    features = lax.all_to_all(pooled, "cache", split_axis=1, concat_axis=0, tiled=True)[:, 0]
    products = jnp.einsum("fne,gne->nfg", features, features, preferred_element_type=jnp.float32)
    interaction = (products / math.sqrt(row_width)).astype(jnp.bfloat16)
    flat_rows = interaction.reshape(interaction.shape[0], -1)
    pre_norm = jnp.dot(flat_rows, top_weight, preferred_element_type=jnp.float32)
    sample_count = pre_norm.shape[0] * lax.axis_size("shard") * caches
    col_mean = lax.psum(jnp.sum(pre_norm, axis=0), ("shard", "cache")) / sample_count
    centered = pre_norm - col_mean
    col_var = lax.psum(jnp.sum(centered * centered, axis=0), ("shard", "cache")) / sample_count
    normed = (pre_norm - col_mean) * lax.rsqrt(col_var + norm_eps) * bn_gain + bn_shift
    top_hidden = jax.nn.relu(normed).astype(jnp.bfloat16)
    logits = jnp.dot(top_hidden, out_weight, preferred_element_type=jnp.float32)
    return (top_hidden, logits)


def solution(mesh):
    return jax.shard_map(
        shards,
        mesh=mesh,
        in_specs=(
            P(("shard", "cache"), None),
            P(("shard", "cache")),
            P("cache", "shard", None),
            P("cache", "shard", None),
            P("cache", "shard"),
            P("shard"),
            P(),
            P(),
            P(),
            P(),
        ),
        out_specs=(P(("shard", "cache"), None), P(("shard", "cache"))),
        check_vma=False,
    )
```

```python
import functools
import math

import jax
import jax.numpy as jnp
from jax import lax
from jax.experimental import pallas as pl
from jax.experimental.pallas import tpu as pltpu
from jax.sharding import PartitionSpec as P

norm_eps = 1e-05


def pool_kernel(order_ref, ids_ref, counts_ref, slots_ref, hot_ref, own_ref, out_ref, acc_ref):
    step = pl.program_id(0)
    block = order_ref[step]
    list_len = slots_ref.shape[1]
    hot_count = hot_ref.shape[0] // 128
    own_count = own_ref.shape[0] // 128
    slots = slots_ref[0]
    row_iota = lax.broadcasted_iota(jnp.int32, (128, 128), 0)
    acc_ref[...] = jnp.zeros(acc_ref.shape, jnp.float32)

    def place(k, carry):
        shifted = slots - k * 128
        hits = jnp.zeros((128, 128), jnp.float32)
        for entry in range(list_len):
            hits = hits + (shifted[entry : entry + 1, :] == row_iota).astype(jnp.float32)
        name = jnp.clip(ids_ref[block * list_len + k], 0, hot_count + own_count - 1)
        hot_start = pl.multiple_of(jnp.minimum(name, hot_count - 1) * 128, 128)
        own_start = pl.multiple_of(jnp.maximum(name - hot_count, 0) * 128, 128)
        rows = jnp.where(
            name < hot_count,
            hot_ref[pl.ds(hot_start, 128), :],
            own_ref[pl.ds(own_start, 128), :],
        )
        acc_ref[...] += lax.dot_general(
            hits.astype(jnp.bfloat16),
            rows,
            (((0,), (0,)), ((), ())),
            preferred_element_type=jnp.float32,
        )
        return carry

    count = jnp.clip(counts_ref[block], 0, list_len)
    lax.fori_loop(0, count, place, 0)
    out_ref[...] = acc_ref[...].astype(out_ref.dtype)


def pool(order, ids, counts, slots_t, hot, own):
    blocks, bag_len, _ = slots_t.shape
    width = hot.shape[1]
    grid_spec = pltpu.PrefetchScalarGridSpec(
        num_scalar_prefetch=3,
        grid=(blocks,),
        in_specs=[
            pl.BlockSpec((1, bag_len, 128), lambda i, o, d, c: (o[i], 0, 0)),
            pl.BlockSpec(hot.shape, lambda i, o, d, c: (0, 0)),
            pl.BlockSpec(own.shape, lambda i, o, d, c: (0, 0)),
        ],
        out_specs=pl.BlockSpec((128, width), lambda i, o, d, c: (i, 0)),
        scratch_shapes=[pltpu.VMEM((128, width), jnp.float32)],
    )
    return pl.pallas_call(
        pool_kernel,
        grid_spec=grid_spec,
        out_shape=jax.ShapeDtypeStruct((blocks * 128, width), jnp.bfloat16),
        compiler_params=pltpu.CompilerParams(
            dimension_semantics=("arbitrary",), vmem_limit_bytes=40 * 1024 * 1024
        ),
    )(order, ids, counts, slots_t, hot, own)


def merge_pair(stats, axis, size, bit, count):
    mean, m2 = stats[0], stats[1]
    other = lax.ppermute(stats, axis, [(i, i ^ bit) for i in range(size)])
    gap = mean - other[0]
    merged_mean = (mean + other[0]) * 0.5
    merged_m2 = (m2 + other[1]) + gap * gap * (count * 0.5)
    return jnp.stack([merged_mean, merged_m2])


def merge_three(stats, axis, size, stride, count):
    place = lax.axis_index(axis) // stride
    back = lax.ppermute(stats, axis, [(i, (i + stride) % size) for i in range(size)])
    ahead = lax.ppermute(stats, axis, [(i, (i + 2 * stride) % size) for i in range(size)])
    parts = []
    for pos in range(3):
        parts.append(
            jnp.where(place == pos, stats, jnp.where((place + 2) % 3 == pos, back, ahead))
        )
    mean = (parts[0][0] + parts[1][0] + parts[2][0]) / 3.0
    m2 = parts[0][1] + parts[1][1] + parts[2][1]
    spread = (parts[0][0] - mean) ** 2 + (parts[1][0] - mean) ** 2 + (parts[2][0] - mean) ** 2
    return jnp.stack([mean, m2 + spread * count])


def column_stats(values, axes):
    count = float(values.shape[0])
    mean = jnp.sum(values, axis=0) / count
    centered = values - mean
    stats = jnp.stack([mean, jnp.sum(centered * centered, axis=0)])
    for axis, size in axes:
        bit = 1
        while size % (2 * bit) == 0:
            stats = merge_pair(stats, axis, size, bit, count)
            count *= 2
            bit *= 2
        rest = size // bit
        if rest == 3:
            stats = merge_three(stats, axis, size, bit, count)
            count *= 3
        elif rest != 1:
            raise ValueError("axis size")
    return stats[0], stats[1]


def shards(
    table,
    panel_ids,
    bag_slots,
    block_ids,
    bag_counts,
    dense_owner,
    top_weight,
    bn_gain,
    bn_shift,
    out_weight,
):
    row_width = table.shape[1]
    caches = lax.axis_size("cache")
    feat_dev, group_samp, bag_len = bag_slots.shape
    samp_dev = group_samp // caches
    owner_blocks = samp_dev // 128
    group_blocks = group_samp // 128
    blocks_dev = feat_dev * group_blocks
    list_len = block_ids.shape[2]
    hot_rows = jnp.take(table.reshape(-1, 128, row_width), panel_ids, axis=0).reshape(-1, row_width)
    cache_ids = jnp.arange(caches, dtype=jnp.int32)
    owner_match = dense_owner[None, :] == cache_ids[:, None]
    inverse = jnp.sum(jnp.where(owner_match, cache_ids[None, :], 0), axis=1)
    block_number = jnp.arange(blocks_dev, dtype=jnp.int32)
    feature_part = block_number // group_blocks
    within_group = block_number % group_blocks
    source_block = (
        feature_part * group_blocks
        + inverse[within_group // owner_blocks] * owner_blocks
        + within_group % owner_blocks
    ).astype(jnp.int32)
    slots_t = jnp.swapaxes(bag_slots.reshape(blocks_dev, 128, bag_len), 1, 2)
    ids = block_ids.reshape(blocks_dev * list_len).astype(jnp.int32)
    counts = bag_counts.reshape(blocks_dev).astype(jnp.int32)
    gathered = lax.all_gather(hot_rows, "cache", axis=0, tiled=True)
    pooled = pool(source_block, ids, counts, slots_t, gathered, table)
    pooled = pooled.reshape(feat_dev, caches, samp_dev, row_width)
    features = lax.all_to_all(pooled, "cache", split_axis=1, concat_axis=0, tiled=True)[:, 0]
    products = jnp.einsum("fne,gne->nfg", features, features, preferred_element_type=jnp.float32)
    interaction = (products / math.sqrt(row_width)).astype(jnp.bfloat16)
    flat_rows = interaction.reshape(interaction.shape[0], -1)
    pre_norm = jnp.dot(flat_rows, top_weight, preferred_element_type=jnp.float32)
    col_mean, col_m2 = column_stats(pre_norm, (("cache", caches), ("shard", lax.axis_size("shard"))))
    col_var = col_m2 / (pre_norm.shape[0] * lax.axis_size("shard") * caches)
    normed = (pre_norm - col_mean) * lax.rsqrt(col_var + norm_eps) * bn_gain + bn_shift
    top_hidden = jax.nn.relu(normed).astype(jnp.bfloat16)
    logits = jnp.dot(top_hidden, out_weight, preferred_element_type=jnp.float32)
    return (top_hidden, logits)


def solution(mesh):
    return jax.shard_map(
        shards,
        mesh=mesh,
        in_specs=(
            P(("shard", "cache"), None),
            P(("shard", "cache")),
            P("cache", "shard", None),
            P("cache", "shard", None),
            P("cache", "shard"),
            P("shard"),
            P(),
            P(),
            P(),
            P(),
        ),
        out_specs=(P(("shard", "cache"), None), P(("shard", "cache"))),
        check_vma=False,
    )
```

```python
import functools
import math

import jax
import jax.numpy as jnp
from jax import lax
from jax.experimental import pallas as pl
from jax.experimental.pallas import tpu as pltpu
from jax.sharding import PartitionSpec as P

norm_eps = 1e-05


def pool_kernel(order_ref, ids_ref, counts_ref, slots_ref, hot_ref, own_ref, out_ref, hits_ref, cols_ref):
    step = pl.program_id(0)
    block = order_ref[step]
    list_len = slots_ref.shape[1]
    hot_devices, _, hot_width = hot_ref.shape
    hot_dev = hot_width // 128
    hot_count = hot_devices * hot_dev
    own_count = own_ref.shape[1] // 128
    slots = slots_ref[0]
    row_iota = lax.broadcasted_iota(jnp.int32, (128, 128), 0)

    @pl.when(step == 0)
    def _():
        cols_ref[...] = jnp.zeros(cols_ref.shape, cols_ref.dtype)

    def place(k, carry):
        shifted = slots - k * 128
        hits = jnp.zeros((128, 128), jnp.float32)
        for entry in range(list_len):
            hits = hits + (shifted[entry : entry + 1, :] == row_iota).astype(jnp.float32)
        start = pl.multiple_of(k * 128, 128)
        hits_ref[pl.ds(start, 128), :] = hits.astype(hits_ref.dtype)
        name = jnp.clip(ids_ref[block * list_len + k], 0, hot_count + own_count - 1)
        hot_name = jnp.minimum(name, hot_count - 1)
        hot_start = pl.multiple_of((hot_name % hot_dev) * 128, 128)
        own_start = pl.multiple_of(jnp.maximum(name - hot_count, 0) * 128, 128)

        @pl.when(name < hot_count)
        def _():
            cols_ref[:, pl.ds(start, 128)] = hot_ref[hot_name // hot_dev, :, pl.ds(hot_start, 128)]

        @pl.when(name >= hot_count)
        def _():
            cols_ref[:, pl.ds(start, 128)] = own_ref[:, pl.ds(own_start, 128)]

        return carry

    def unused(k, carry):
        start = pl.multiple_of(k * 128, 128)
        hits_ref[pl.ds(start, 128), :] = jnp.zeros((128, 128), hits_ref.dtype)
        return carry

    count = jnp.clip(counts_ref[block], 0, list_len)
    lax.fori_loop(0, count, place, 0)
    lax.fori_loop(count, list_len, unused, 0)
    total = jnp.dot(cols_ref[...], hits_ref[...], preferred_element_type=jnp.float32)
    out_ref[...] = total.T.astype(out_ref.dtype)


def pool(order, ids, counts, slots_t, hot_t, own_t):
    blocks, bag_len, _ = slots_t.shape
    width = own_t.shape[0]
    grid_spec = pltpu.PrefetchScalarGridSpec(
        num_scalar_prefetch=3,
        grid=(blocks,),
        in_specs=[
            pl.BlockSpec((1, bag_len, 128), lambda i, o, d, c: (o[i], 0, 0)),
            pl.BlockSpec(hot_t.shape, lambda i, o, d, c: (0, 0, 0)),
            pl.BlockSpec(own_t.shape, lambda i, o, d, c: (0, 0)),
        ],
        out_specs=pl.BlockSpec((128, width), lambda i, o, d, c: (i, 0)),
        scratch_shapes=[
            pltpu.VMEM((bag_len * 128, 128), jnp.bfloat16),
            pltpu.VMEM((width, bag_len * 128), jnp.bfloat16),
        ],
    )
    return pl.pallas_call(
        pool_kernel,
        grid_spec=grid_spec,
        out_shape=jax.ShapeDtypeStruct((blocks * 128, width), jnp.bfloat16),
        compiler_params=pltpu.CompilerParams(
            dimension_semantics=("arbitrary",), vmem_limit_bytes=40 * 1024 * 1024
        ),
    )(order, ids, counts, slots_t, hot_t, own_t)

def merge_pair(stats, axis, size, bit, count):
    mean, m2 = stats[0], stats[1]
    other = lax.ppermute(stats, axis, [(i, i ^ bit) for i in range(size)])
    gap = mean - other[0]
    merged_mean = (mean + other[0]) * 0.5
    merged_m2 = (m2 + other[1]) + gap * gap * (count * 0.5)
    return jnp.stack([merged_mean, merged_m2])


def merge_three(stats, axis, size, stride, count):
    place = lax.axis_index(axis) // stride
    back = lax.ppermute(stats, axis, [(i, (i + stride) % size) for i in range(size)])
    ahead = lax.ppermute(stats, axis, [(i, (i + 2 * stride) % size) for i in range(size)])
    parts = []
    for pos in range(3):
        parts.append(
            jnp.where(place == pos, stats, jnp.where((place + 2) % 3 == pos, back, ahead))
        )
    mean = (parts[0][0] + parts[1][0] + parts[2][0]) / 3.0
    m2 = parts[0][1] + parts[1][1] + parts[2][1]
    spread = (parts[0][0] - mean) ** 2 + (parts[1][0] - mean) ** 2 + (parts[2][0] - mean) ** 2
    return jnp.stack([mean, m2 + spread * count])


def column_stats(values, axes):
    count = float(values.shape[0])
    mean = jnp.sum(values, axis=0) / count
    centered = values - mean
    stats = jnp.stack([mean, jnp.sum(centered * centered, axis=0)])
    for axis, size in axes:
        bit = 1
        while size % (2 * bit) == 0:
            stats = merge_pair(stats, axis, size, bit, count)
            count *= 2
            bit *= 2
        rest = size // bit
        if rest == 3:
            stats = merge_three(stats, axis, size, bit, count)
            count *= 3
        elif rest != 1:
            raise ValueError("axis size")
    return stats[0], stats[1]


def shards(
    table,
    panel_ids,
    bag_slots,
    block_ids,
    bag_counts,
    dense_owner,
    top_weight,
    bn_gain,
    bn_shift,
    out_weight,
):
    row_width = table.shape[1]
    caches = lax.axis_size("cache")
    feat_dev, group_samp, bag_len = bag_slots.shape
    samp_dev = group_samp // caches
    owner_blocks = samp_dev // 128
    group_blocks = group_samp // 128
    blocks_dev = feat_dev * group_blocks
    list_len = block_ids.shape[2]
    hot_rows = jnp.take(table.reshape(-1, 128, row_width), panel_ids, axis=0).reshape(-1, row_width)
    cache_ids = jnp.arange(caches, dtype=jnp.int32)
    owner_match = dense_owner[None, :] == cache_ids[:, None]
    inverse = jnp.sum(jnp.where(owner_match, cache_ids[None, :], 0), axis=1)
    block_number = jnp.arange(blocks_dev, dtype=jnp.int32)
    feature_part = block_number // group_blocks
    within_group = block_number % group_blocks
    source_block = (
        feature_part * group_blocks
        + inverse[within_group // owner_blocks] * owner_blocks
        + within_group % owner_blocks
    ).astype(jnp.int32)
    slots_t = jnp.swapaxes(bag_slots.reshape(blocks_dev, 128, bag_len), 1, 2)
    ids = block_ids.reshape(blocks_dev * list_len).astype(jnp.int32)
    counts = bag_counts.reshape(blocks_dev).astype(jnp.int32)
    gathered = lax.all_gather(hot_rows.T, "cache", axis=0)
    pooled = pool(source_block, ids, counts, slots_t, gathered, table.T)
    pooled = pooled.reshape(feat_dev, caches, samp_dev, row_width)
    features = lax.all_to_all(pooled, "cache", split_axis=1, concat_axis=0, tiled=True)[:, 0]
    products = jnp.einsum("fne,gne->nfg", features, features, preferred_element_type=jnp.float32)
    interaction = (products / math.sqrt(row_width)).astype(jnp.bfloat16)
    flat_rows = interaction.reshape(interaction.shape[0], -1)
    pre_norm = jnp.dot(flat_rows, top_weight, preferred_element_type=jnp.float32)
    col_mean, col_m2 = column_stats(pre_norm, (("cache", caches), ("shard", lax.axis_size("shard"))))
    col_var = col_m2 / (pre_norm.shape[0] * lax.axis_size("shard") * caches)
    normed = (pre_norm - col_mean) * lax.rsqrt(col_var + norm_eps) * bn_gain + bn_shift
    top_hidden = jax.nn.relu(normed).astype(jnp.bfloat16)
    logits = jnp.dot(top_hidden, out_weight, preferred_element_type=jnp.float32)
    return (top_hidden, logits)


def solution(mesh):
    return jax.shard_map(
        shards,
        mesh=mesh,
        in_specs=(
            P(("shard", "cache"), None),
            P(("shard", "cache")),
            P("cache", "shard", None),
            P("cache", "shard", None),
            P("cache", "shard"),
            P("shard"),
            P(),
            P(),
            P(),
            P(),
        ),
        out_specs=(P(("shard", "cache"), None), P(("shard", "cache"))),
        check_vma=False,
    )
```

```python
import functools
import math

import jax
import jax.numpy as jnp
from jax import lax
from jax.experimental import pallas as pl
from jax.experimental.pallas import tpu as pltpu
from jax.sharding import PartitionSpec as P

norm_eps = 1e-05


def pool_kernel(order_ref, ids_ref, counts_ref, slots_ref, hot_ref, own_ref, out_ref, hits_ref, cols_ref, rows_ref):
    step = pl.program_id(0)
    block = order_ref[step]
    list_len = slots_ref.shape[1]
    hot_devices, _, hot_width = hot_ref.shape
    hot_dev = hot_width // 128
    hot_count = hot_devices * hot_dev
    own_count = own_ref.shape[1] // 128
    slots = slots_ref[0]
    row_iota = lax.broadcasted_iota(jnp.int32, (128, 128), 0)

    @pl.when(step == 0)
    def _():
        cols_ref[...] = jnp.zeros(cols_ref.shape, cols_ref.dtype)

    low = slots % 128
    high = slots // 128
    for entry in range(list_len):
        rows_ref[entry] = (low[entry : entry + 1, :] == row_iota).astype(jnp.float32)

    def place(k, carry):
        hits = jnp.zeros((128, 128), jnp.float32)
        for entry in range(list_len):
            hits = hits + jnp.where(high[entry : entry + 1, :] == k, rows_ref[entry], 0.0)
        start = pl.multiple_of(k * 128, 128)
        hits_ref[pl.ds(start, 128), :] = hits.astype(hits_ref.dtype)
        name = jnp.clip(ids_ref[block * list_len + k], 0, hot_count + own_count - 1)
        hot_name = jnp.minimum(name, hot_count - 1)
        hot_start = pl.multiple_of((hot_name % hot_dev) * 128, 128)
        own_start = pl.multiple_of(jnp.maximum(name - hot_count, 0) * 128, 128)

        @pl.when(name < hot_count)
        def _():
            cols_ref[:, pl.ds(start, 128)] = hot_ref[hot_name // hot_dev, :, pl.ds(hot_start, 128)]

        @pl.when(name >= hot_count)
        def _():
            cols_ref[:, pl.ds(start, 128)] = own_ref[:, pl.ds(own_start, 128)]

        return carry

    def unused(k, carry):
        start = pl.multiple_of(k * 128, 128)
        hits_ref[pl.ds(start, 128), :] = jnp.zeros((128, 128), hits_ref.dtype)
        return carry

    count = jnp.clip(counts_ref[block], 0, list_len)
    lax.fori_loop(0, count, place, 0)
    lax.fori_loop(count, list_len, unused, 0)
    total = jnp.dot(cols_ref[...], hits_ref[...], preferred_element_type=jnp.float32)
    out_ref[...] = total.T.astype(out_ref.dtype)


def pool(order, ids, counts, slots_t, hot_t, own_t):
    blocks, bag_len, _ = slots_t.shape
    width = own_t.shape[0]
    grid_spec = pltpu.PrefetchScalarGridSpec(
        num_scalar_prefetch=3,
        grid=(blocks,),
        in_specs=[
            pl.BlockSpec((1, bag_len, 128), lambda i, o, d, c: (o[i], 0, 0)),
            pl.BlockSpec(hot_t.shape, lambda i, o, d, c: (0, 0, 0)),
            pl.BlockSpec(own_t.shape, lambda i, o, d, c: (0, 0)),
        ],
        out_specs=pl.BlockSpec((128, width), lambda i, o, d, c: (i, 0)),
        scratch_shapes=[
            pltpu.VMEM((bag_len * 128, 128), jnp.bfloat16),
            pltpu.VMEM((width, bag_len * 128), jnp.bfloat16),
            pltpu.VMEM((bag_len, 128, 128), jnp.float32),
        ],
    )
    return pl.pallas_call(
        pool_kernel,
        grid_spec=grid_spec,
        out_shape=jax.ShapeDtypeStruct((blocks * 128, width), jnp.bfloat16),
        compiler_params=pltpu.CompilerParams(
            dimension_semantics=("arbitrary",), vmem_limit_bytes=40 * 1024 * 1024
        ),
    )(order, ids, counts, slots_t, hot_t, own_t)

def merge_pair(stats, axis, size, bit, count):
    mean, m2 = stats[0], stats[1]
    other = lax.ppermute(stats, axis, [(i, i ^ bit) for i in range(size)])
    gap = mean - other[0]
    merged_mean = (mean + other[0]) * 0.5
    merged_m2 = (m2 + other[1]) + gap * gap * (count * 0.5)
    return jnp.stack([merged_mean, merged_m2])


def merge_three(stats, axis, size, stride, count):
    place = lax.axis_index(axis) // stride
    back = lax.ppermute(stats, axis, [(i, (i + stride) % size) for i in range(size)])
    ahead = lax.ppermute(stats, axis, [(i, (i + 2 * stride) % size) for i in range(size)])
    parts = []
    for pos in range(3):
        parts.append(
            jnp.where(place == pos, stats, jnp.where((place + 2) % 3 == pos, back, ahead))
        )
    mean = (parts[0][0] + parts[1][0] + parts[2][0]) / 3.0
    m2 = parts[0][1] + parts[1][1] + parts[2][1]
    spread = (parts[0][0] - mean) ** 2 + (parts[1][0] - mean) ** 2 + (parts[2][0] - mean) ** 2
    return jnp.stack([mean, m2 + spread * count])


def column_stats(values, axes):
    count = float(values.shape[0])
    mean = jnp.sum(values, axis=0) / count
    centered = values - mean
    stats = jnp.stack([mean, jnp.sum(centered * centered, axis=0)])
    for axis, size in axes:
        bit = 1
        while size % (2 * bit) == 0:
            stats = merge_pair(stats, axis, size, bit, count)
            count *= 2
            bit *= 2
        rest = size // bit
        if rest == 3:
            stats = merge_three(stats, axis, size, bit, count)
            count *= 3
        elif rest != 1:
            raise ValueError("axis size")
    return stats[0], stats[1]


def shards(
    table,
    panel_ids,
    bag_slots,
    block_ids,
    bag_counts,
    dense_owner,
    top_weight,
    bn_gain,
    bn_shift,
    out_weight,
):
    row_width = table.shape[1]
    caches = lax.axis_size("cache")
    feat_dev, group_samp, bag_len = bag_slots.shape
    samp_dev = group_samp // caches
    owner_blocks = samp_dev // 128
    group_blocks = group_samp // 128
    blocks_dev = feat_dev * group_blocks
    list_len = block_ids.shape[2]
    hot_rows = jnp.take(table.reshape(-1, 128, row_width), panel_ids, axis=0).reshape(-1, row_width)
    cache_ids = jnp.arange(caches, dtype=jnp.int32)
    owner_match = dense_owner[None, :] == cache_ids[:, None]
    inverse = jnp.sum(jnp.where(owner_match, cache_ids[None, :], 0), axis=1)
    block_number = jnp.arange(blocks_dev, dtype=jnp.int32)
    feature_part = block_number // group_blocks
    within_group = block_number % group_blocks
    source_block = (
        feature_part * group_blocks
        + inverse[within_group // owner_blocks] * owner_blocks
        + within_group % owner_blocks
    ).astype(jnp.int32)
    slots_t = jnp.swapaxes(bag_slots.reshape(blocks_dev, 128, bag_len), 1, 2)
    ids = block_ids.reshape(blocks_dev * list_len).astype(jnp.int32)
    counts = bag_counts.reshape(blocks_dev).astype(jnp.int32)
    gathered = lax.all_gather(hot_rows.T, "cache", axis=0)
    pooled = pool(source_block, ids, counts, slots_t, gathered, table.T)
    pooled = pooled.reshape(feat_dev, caches, samp_dev, row_width)
    features = lax.all_to_all(pooled, "cache", split_axis=1, concat_axis=0, tiled=True)[:, 0]
    products = jnp.einsum("fne,gne->nfg", features, features, preferred_element_type=jnp.float32)
    interaction = (products / math.sqrt(row_width)).astype(jnp.bfloat16)
    flat_rows = interaction.reshape(interaction.shape[0], -1)
    pre_norm = jnp.dot(flat_rows, top_weight, preferred_element_type=jnp.float32)
    col_mean, col_m2 = column_stats(pre_norm, (("cache", caches), ("shard", lax.axis_size("shard"))))
    col_var = col_m2 / (pre_norm.shape[0] * lax.axis_size("shard") * caches)
    normed = (pre_norm - col_mean) * lax.rsqrt(col_var + norm_eps) * bn_gain + bn_shift
    top_hidden = jax.nn.relu(normed).astype(jnp.bfloat16)
    logits = jnp.dot(top_hidden, out_weight, preferred_element_type=jnp.float32)
    return (top_hidden, logits)


def solution(mesh):
    return jax.shard_map(
        shards,
        mesh=mesh,
        in_specs=(
            P(("shard", "cache"), None),
            P(("shard", "cache")),
            P("cache", "shard", None),
            P("cache", "shard", None),
            P("cache", "shard"),
            P("shard"),
            P(),
            P(),
            P(),
            P(),
        ),
        out_specs=(P(("shard", "cache"), None), P(("shard", "cache"))),
        check_vma=False,
    )
```

```python
import functools
import math

import jax
import jax.numpy as jnp
from jax import lax
from jax.experimental import pallas as pl
from jax.experimental.pallas import tpu as pltpu
from jax.sharding import PartitionSpec as P

norm_eps = 1e-05


def pool_kernel(order_ref, ids_ref, counts_ref, slots_ref, hot_ref, own_ref, out_ref, hits_ref, cols_ref, rows_ref):
    step = pl.program_id(0)
    block = order_ref[step]
    list_len = slots_ref.shape[1]
    hot_devices, _, hot_width = hot_ref.shape
    hot_dev = hot_width // 128
    hot_count = hot_devices * hot_dev
    own_count = own_ref.shape[1] // 128
    slots = slots_ref[0]
    row_iota = lax.broadcasted_iota(jnp.int32, (128, 128), 0)

    @pl.when(step == 0)
    def _():
        cols_ref[...] = jnp.zeros(cols_ref.shape, cols_ref.dtype)

    low = slots % 128
    high = slots // 128
    for entry in range(list_len):
        rows_ref[entry] = (low[entry : entry + 1, :] == row_iota).astype(jnp.float32)

    def place(k, carry):
        hits = jnp.zeros((128, 128), jnp.float32)
        for entry in range(list_len):
            hits = hits + jnp.where(high[entry : entry + 1, :] == k, rows_ref[entry], 0.0)
        start = pl.multiple_of(k * 128, 128)
        hits_ref[pl.ds(start, 128), :] = hits.astype(hits_ref.dtype)
        name = jnp.clip(ids_ref[block * list_len + k], 0, hot_count + own_count - 1)
        hot_name = jnp.minimum(name, hot_count - 1)
        hot_start = pl.multiple_of((hot_name % hot_dev) * 128, 128)
        own_start = pl.multiple_of(jnp.maximum(name - hot_count, 0) * 128, 128)

        @pl.when(name < hot_count)
        def _():
            cols_ref[:, pl.ds(start, 128)] = hot_ref[hot_name // hot_dev, :, pl.ds(hot_start, 128)]

        @pl.when(name >= hot_count)
        def _():
            cols_ref[:, pl.ds(start, 128)] = own_ref[:, pl.ds(own_start, 128)]

        return carry

    def unused(k, carry):
        start = pl.multiple_of(k * 128, 128)
        hits_ref[pl.ds(start, 128), :] = jnp.zeros((128, 128), hits_ref.dtype)
        return carry

    count = jnp.clip(counts_ref[block], 0, list_len)
    lax.fori_loop(0, count, place, 0)
    lax.fori_loop(count, list_len, unused, 0)
    total = jnp.dot(cols_ref[...], hits_ref[...], preferred_element_type=jnp.float32)
    out_ref[...] = total.T.astype(out_ref.dtype)


def pool(order, ids, counts, slots_t, hot_t, own_t):
    blocks, bag_len, _ = slots_t.shape
    width = own_t.shape[0]
    grid_spec = pltpu.PrefetchScalarGridSpec(
        num_scalar_prefetch=3,
        grid=(blocks,),
        in_specs=[
            pl.BlockSpec((1, bag_len, 128), lambda i, o, d, c: (o[i], 0, 0)),
            pl.BlockSpec(hot_t.shape, lambda i, o, d, c: (0, 0, 0)),
            pl.BlockSpec(own_t.shape, lambda i, o, d, c: (0, 0)),
        ],
        out_specs=pl.BlockSpec((128, width), lambda i, o, d, c: (i, 0)),
        scratch_shapes=[
            pltpu.VMEM((bag_len * 128, 128), jnp.bfloat16),
            pltpu.VMEM((width, bag_len * 128), jnp.bfloat16),
            pltpu.VMEM((bag_len, 128, 128), jnp.float32),
        ],
    )
    return pl.pallas_call(
        pool_kernel,
        grid_spec=grid_spec,
        out_shape=jax.ShapeDtypeStruct((blocks * 128, width), jnp.bfloat16),
        compiler_params=pltpu.CompilerParams(
            dimension_semantics=("arbitrary",), vmem_limit_bytes=40 * 1024 * 1024
        ),
    )(order, ids, counts, slots_t, hot_t, own_t)

def merge_pair(stats, axis, size, bit, count):
    mean, m2 = stats[0], stats[1]
    other = lax.ppermute(stats, axis, [(i, i ^ bit) for i in range(size)])
    gap = mean - other[0]
    merged_mean = (mean + other[0]) * 0.5
    merged_m2 = (m2 + other[1]) + gap * gap * (count * 0.5)
    return jnp.stack([merged_mean, merged_m2])


def merge_three(stats, axis, size, stride, count):
    place = lax.axis_index(axis) // stride
    back = lax.ppermute(stats, axis, [(i, (i + stride) % size) for i in range(size)])
    ahead = lax.ppermute(stats, axis, [(i, (i + 2 * stride) % size) for i in range(size)])
    parts = []
    for pos in range(3):
        parts.append(
            jnp.where(place == pos, stats, jnp.where((place + 2) % 3 == pos, back, ahead))
        )
    mean = (parts[0][0] + parts[1][0] + parts[2][0]) / 3.0
    m2 = parts[0][1] + parts[1][1] + parts[2][1]
    spread = (parts[0][0] - mean) ** 2 + (parts[1][0] - mean) ** 2 + (parts[2][0] - mean) ** 2
    return jnp.stack([mean, m2 + spread * count])


def column_stats(values, axes):
    count = float(values.shape[0])
    mean = jnp.sum(values, axis=0) / count
    centered = values - mean
    stats = jnp.stack([mean, jnp.sum(centered * centered, axis=0)])
    for axis, size in axes:
        bit = 1
        while size % (2 * bit) == 0:
            stats = merge_pair(stats, axis, size, bit, count)
            count *= 2
            bit *= 2
        rest = size // bit
        if rest == 3:
            stats = merge_three(stats, axis, size, bit, count)
            count *= 3
        elif rest != 1:
            raise ValueError("axis size")
    return stats[0], stats[1]


def shards(
    table,
    panel_ids,
    bag_slots,
    block_ids,
    bag_counts,
    dense_owner,
    top_weight,
    bn_gain,
    bn_shift,
    out_weight,
):
    row_width = table.shape[1]
    caches = lax.axis_size("cache")
    feat_dev, group_samp, bag_len = bag_slots.shape
    samp_dev = group_samp // caches
    owner_blocks = samp_dev // 128
    group_blocks = group_samp // 128
    blocks_dev = feat_dev * group_blocks
    list_len = block_ids.shape[2]
    cache_ids = jnp.arange(caches, dtype=jnp.int32)
    owner_match = dense_owner[None, :] == cache_ids[:, None]
    inverse = jnp.sum(jnp.where(owner_match, cache_ids[None, :], 0), axis=1)
    block_number = jnp.arange(blocks_dev, dtype=jnp.int32)
    feature_part = block_number // group_blocks
    within_group = block_number % group_blocks
    source_block = (
        feature_part * group_blocks
        + inverse[within_group // owner_blocks] * owner_blocks
        + within_group % owner_blocks
    ).astype(jnp.int32)
    slots_t = jnp.swapaxes(bag_slots.reshape(blocks_dev, 128, bag_len), 1, 2)
    ids = block_ids.reshape(blocks_dev * list_len).astype(jnp.int32)
    counts = bag_counts.reshape(blocks_dev).astype(jnp.int32)
    own_t = table.T
    hot_t = jnp.take(own_t.reshape(row_width, -1, 128), panel_ids, axis=1).reshape(row_width, -1)
    gathered = lax.all_gather(hot_t, "cache", axis=0)
    pooled = pool(source_block, ids, counts, slots_t, gathered, own_t)
    pooled = pooled.reshape(feat_dev, caches, samp_dev, row_width)
    features = lax.all_to_all(pooled, "cache", split_axis=1, concat_axis=0, tiled=True)[:, 0]
    products = jnp.einsum("fne,gne->nfg", features, features, preferred_element_type=jnp.float32)
    interaction = (products / math.sqrt(row_width)).astype(jnp.bfloat16)
    flat_rows = interaction.reshape(interaction.shape[0], -1)
    pre_norm = jnp.dot(flat_rows, top_weight, preferred_element_type=jnp.float32)
    col_mean, col_m2 = column_stats(pre_norm, (("cache", caches), ("shard", lax.axis_size("shard"))))
    col_var = col_m2 / (pre_norm.shape[0] * lax.axis_size("shard") * caches)
    normed = (pre_norm - col_mean) * lax.rsqrt(col_var + norm_eps) * bn_gain + bn_shift
    top_hidden = jax.nn.relu(normed).astype(jnp.bfloat16)
    logits = jnp.dot(top_hidden, out_weight, preferred_element_type=jnp.float32)
    return (top_hidden, logits)


def solution(mesh):
    return jax.shard_map(
        shards,
        mesh=mesh,
        in_specs=(
            P(("shard", "cache"), None),
            P(("shard", "cache")),
            P("cache", "shard", None),
            P("cache", "shard", None),
            P("cache", "shard"),
            P("shard"),
            P(),
            P(),
            P(),
            P(),
        ),
        out_specs=(P(("shard", "cache"), None), P(("shard", "cache"))),
        check_vma=False,
    )
```

```python
import functools
import math

import jax
import jax.numpy as jnp
from jax import lax
from jax.experimental import pallas as pl
from jax.experimental.pallas import tpu as pltpu
from jax.sharding import PartitionSpec as P

norm_eps = 1e-05


def pool_kernel(order_ref, ids_ref, counts_ref, slots_ref, hot_ref, own_ref, out_ref, hits_ref, cols_ref, rows_ref):
    step = pl.program_id(0)
    block = order_ref[step]
    list_len = slots_ref.shape[1]
    hot_devices, _, hot_width = hot_ref.shape
    hot_dev = hot_width // 128
    hot_count = hot_devices * hot_dev
    own_count = own_ref.shape[1] // 128
    slots = slots_ref[0]
    row_iota = lax.broadcasted_iota(jnp.int32, (128, 128), 0)

    @pl.when(step == 0)
    def _():
        cols_ref[...] = jnp.zeros(cols_ref.shape, cols_ref.dtype)

    low = slots % 128
    high = slots // 128
    for entry in range(list_len):
        rows_ref[entry] = (low[entry : entry + 1, :] == row_iota).astype(jnp.float32)

    def place(k, carry):
        hits = jnp.zeros((128, 128), jnp.float32)
        for entry in range(list_len):
            hits = hits + jnp.where(high[entry : entry + 1, :] == k, rows_ref[entry], 0.0)
        start = pl.multiple_of(k * 128, 128)
        hits_ref[pl.ds(start, 128), :] = hits.astype(hits_ref.dtype)
        name = jnp.clip(ids_ref[block * list_len + k], 0, hot_count + own_count - 1)
        hot_name = jnp.minimum(name, hot_count - 1)
        hot_start = pl.multiple_of((hot_name % hot_dev) * 128, 128)
        own_start = pl.multiple_of(jnp.maximum(name - hot_count, 0) * 128, 128)

        @pl.when(name < hot_count)
        def _():
            cols_ref[:, pl.ds(start, 128)] = hot_ref[hot_name // hot_dev, :, pl.ds(hot_start, 128)]

        @pl.when(name >= hot_count)
        def _():
            cols_ref[:, pl.ds(start, 128)] = own_ref[:, pl.ds(own_start, 128)]

        return carry

    def unused(k, carry):
        start = pl.multiple_of(k * 128, 128)
        hits_ref[pl.ds(start, 128), :] = jnp.zeros((128, 128), hits_ref.dtype)
        return carry

    count = jnp.clip(counts_ref[block], 0, list_len)
    lax.fori_loop(0, count, place, 0)
    lax.fori_loop(count, list_len, unused, 0)
    total = jnp.dot(cols_ref[...], hits_ref[...], preferred_element_type=jnp.float32)
    out_ref[...] = total.T.astype(out_ref.dtype)


def pool(order, ids, counts, slots_t, hot_t, own_t):
    blocks = order.shape[0]
    bag_len = slots_t.shape[1]
    width = own_t.shape[0]
    grid_spec = pltpu.PrefetchScalarGridSpec(
        num_scalar_prefetch=3,
        grid=(blocks,),
        in_specs=[
            pl.BlockSpec((1, bag_len, 128), lambda i, o, d, c: (o[i], 0, 0)),
            pl.BlockSpec(hot_t.shape, lambda i, o, d, c: (0, 0, 0)),
            pl.BlockSpec(own_t.shape, lambda i, o, d, c: (0, 0)),
        ],
        out_specs=pl.BlockSpec((128, width), lambda i, o, d, c: (i, 0)),
        scratch_shapes=[
            pltpu.VMEM((bag_len * 128, 128), jnp.bfloat16),
            pltpu.VMEM((width, bag_len * 128), jnp.bfloat16),
            pltpu.VMEM((bag_len, 128, 128), jnp.float32),
        ],
    )
    return pl.pallas_call(
        pool_kernel,
        grid_spec=grid_spec,
        out_shape=jax.ShapeDtypeStruct((blocks * 128, width), jnp.bfloat16),
        compiler_params=pltpu.CompilerParams(
            dimension_semantics=("arbitrary",), vmem_limit_bytes=40 * 1024 * 1024
        ),
    )(order, ids, counts, slots_t, hot_t, own_t)

def merge_pair(stats, axis, size, bit, count):
    mean, m2 = stats[0], stats[1]
    other = lax.ppermute(stats, axis, [(i, i ^ bit) for i in range(size)])
    gap = mean - other[0]
    merged_mean = (mean + other[0]) * 0.5
    merged_m2 = (m2 + other[1]) + gap * gap * (count * 0.5)
    return jnp.stack([merged_mean, merged_m2])


def merge_three(stats, axis, size, stride, count):
    place = lax.axis_index(axis) // stride
    back = lax.ppermute(stats, axis, [(i, (i + stride) % size) for i in range(size)])
    ahead = lax.ppermute(stats, axis, [(i, (i + 2 * stride) % size) for i in range(size)])
    parts = []
    for pos in range(3):
        parts.append(
            jnp.where(place == pos, stats, jnp.where((place + 2) % 3 == pos, back, ahead))
        )
    mean = (parts[0][0] + parts[1][0] + parts[2][0]) / 3.0
    m2 = parts[0][1] + parts[1][1] + parts[2][1]
    spread = (parts[0][0] - mean) ** 2 + (parts[1][0] - mean) ** 2 + (parts[2][0] - mean) ** 2
    return jnp.stack([mean, m2 + spread * count])


def column_stats(values, axes):
    count = float(values.shape[0])
    mean = jnp.sum(values, axis=0) / count
    centered = values - mean
    stats = jnp.stack([mean, jnp.sum(centered * centered, axis=0)])
    for axis, size in axes:
        bit = 1
        while size % (2 * bit) == 0:
            stats = merge_pair(stats, axis, size, bit, count)
            count *= 2
            bit *= 2
        rest = size // bit
        if rest == 3:
            stats = merge_three(stats, axis, size, bit, count)
            count *= 3
        elif rest != 1:
            raise ValueError("axis size")
    return stats[0], stats[1]


def shards(
    table,
    panel_ids,
    bag_slots,
    block_ids,
    bag_counts,
    dense_owner,
    top_weight,
    bn_gain,
    bn_shift,
    out_weight,
):
    row_width = table.shape[1]
    caches = lax.axis_size("cache")
    feat_dev, group_samp, bag_len = bag_slots.shape
    samp_dev = group_samp // caches
    owner_blocks = samp_dev // 128
    group_blocks = group_samp // 128
    blocks_dev = feat_dev * group_blocks
    list_len = block_ids.shape[2]
    cache_ids = jnp.arange(caches, dtype=jnp.int32)
    owner_match = dense_owner[None, :] == cache_ids[:, None]
    inverse = jnp.sum(jnp.where(owner_match, cache_ids[None, :], 0), axis=1)
    block_number = jnp.arange(blocks_dev, dtype=jnp.int32)
    feature_part = block_number // group_blocks
    within_group = block_number % group_blocks
    source_block = (
        feature_part * group_blocks
        + inverse[within_group // owner_blocks] * owner_blocks
        + within_group % owner_blocks
    ).astype(jnp.int32)
    slots_t = jnp.swapaxes(bag_slots.reshape(blocks_dev, 128, bag_len), 1, 2)
    ids = block_ids.reshape(blocks_dev * list_len).astype(jnp.int32)
    counts = bag_counts.reshape(blocks_dev).astype(jnp.int32)
    own_t = table.T
    hot_t = jnp.take(own_t.reshape(row_width, -1, 128), panel_ids, axis=1).reshape(row_width, -1)
    gathered = lax.all_gather(hot_t, "cache", axis=0)
    halves = []
    for half in range(owner_blocks):
        pooled = pool(source_block[half::owner_blocks], ids, counts, slots_t, gathered, own_t)
        pooled = pooled.reshape(feat_dev, caches, 128, row_width)
        halves.append(lax.all_to_all(pooled, "cache", split_axis=1, concat_axis=0, tiled=True)[:, 0])
    features = jnp.concatenate(halves, axis=1)
    products = jnp.einsum("fne,gne->nfg", features, features, preferred_element_type=jnp.float32)
    interaction = (products / math.sqrt(row_width)).astype(jnp.bfloat16)
    flat_rows = interaction.reshape(interaction.shape[0], -1)
    pre_norm = jnp.dot(flat_rows, top_weight, preferred_element_type=jnp.float32)
    col_mean, col_m2 = column_stats(pre_norm, (("cache", caches), ("shard", lax.axis_size("shard"))))
    col_var = col_m2 / (pre_norm.shape[0] * lax.axis_size("shard") * caches)
    normed = (pre_norm - col_mean) * lax.rsqrt(col_var + norm_eps) * bn_gain + bn_shift
    top_hidden = jax.nn.relu(normed).astype(jnp.bfloat16)
    logits = jnp.dot(top_hidden, out_weight, preferred_element_type=jnp.float32)
    return (top_hidden, logits)


def solution(mesh):
    return jax.shard_map(
        shards,
        mesh=mesh,
        in_specs=(
            P(("shard", "cache"), None),
            P(("shard", "cache")),
            P("cache", "shard", None),
            P("cache", "shard", None),
            P("cache", "shard"),
            P("shard"),
            P(),
            P(),
            P(),
            P(),
        ),
        out_specs=(P(("shard", "cache"), None), P(("shard", "cache"))),
        check_vma=False,
    )
```

```python
import functools
import math

import jax
import jax.numpy as jnp
from jax import lax
from jax.experimental import pallas as pl
from jax.experimental.pallas import tpu as pltpu
from jax.sharding import PartitionSpec as P

norm_eps = 1e-05


def pool_kernel(order_ref, ids_ref, counts_ref, slots_ref, hot_ref, own_ref, out_ref, hits_ref, cols_ref, rows_ref):
    step = pl.program_id(0)
    block = order_ref[step]
    list_len = slots_ref.shape[1]
    hot_devices, _, hot_width = hot_ref.shape
    hot_dev = hot_width // 128
    hot_count = hot_devices * hot_dev
    own_count = own_ref.shape[1] // 128
    slots = slots_ref[0]
    row_iota = lax.broadcasted_iota(jnp.int32, (128, 128), 0)

    @pl.when(step == 0)
    def _():
        cols_ref[...] = jnp.zeros(cols_ref.shape, cols_ref.dtype)

    low = slots % 128
    high = slots // 128
    for entry in range(list_len):
        rows_ref[entry] = (low[entry : entry + 1, :] == row_iota).astype(jnp.float32)

    def place(k, carry):
        hits = jnp.zeros((128, 128), jnp.float32)
        for entry in range(list_len):
            hits = hits + jnp.where(high[entry : entry + 1, :] == k, rows_ref[entry], 0.0)
        start = pl.multiple_of(k * 128, 128)
        hits_ref[pl.ds(start, 128), :] = hits.astype(hits_ref.dtype)
        name = jnp.clip(ids_ref[block * list_len + k], 0, hot_count + own_count - 1)
        hot_name = jnp.minimum(name, hot_count - 1)
        hot_start = pl.multiple_of((hot_name % hot_dev) * 128, 128)
        own_start = pl.multiple_of(jnp.maximum(name - hot_count, 0) * 128, 128)

        @pl.when(name < hot_count)
        def _():
            cols_ref[:, pl.ds(start, 128)] = hot_ref[hot_name // hot_dev, :, pl.ds(hot_start, 128)]

        @pl.when(name >= hot_count)
        def _():
            cols_ref[:, pl.ds(start, 128)] = own_ref[:, pl.ds(own_start, 128)]

        return carry

    def unused(k, carry):
        start = pl.multiple_of(k * 128, 128)
        hits_ref[pl.ds(start, 128), :] = jnp.zeros((128, 128), hits_ref.dtype)
        return carry

    count = jnp.clip(counts_ref[block], 0, list_len)
    lax.fori_loop(0, count, place, 0)
    lax.fori_loop(count, list_len, unused, 0)
    total = jnp.dot(cols_ref[...], hits_ref[...], preferred_element_type=jnp.float32)
    out_ref[...] = total.T.astype(out_ref.dtype)


def pool(order, ids, counts, slots_t, hot_t, own_t):
    blocks = order.shape[0]
    bag_len = slots_t.shape[1]
    width = own_t.shape[0]
    grid_spec = pltpu.PrefetchScalarGridSpec(
        num_scalar_prefetch=3,
        grid=(blocks,),
        in_specs=[
            pl.BlockSpec((1, bag_len, 128), lambda i, o, d, c: (o[i], 0, 0)),
            pl.BlockSpec(hot_t.shape, lambda i, o, d, c: (0, 0, 0)),
            pl.BlockSpec(own_t.shape, lambda i, o, d, c: (0, 0)),
        ],
        out_specs=pl.BlockSpec((128, width), lambda i, o, d, c: (i, 0)),
        scratch_shapes=[
            pltpu.VMEM((bag_len * 128, 128), jnp.bfloat16),
            pltpu.VMEM((width, bag_len * 128), jnp.bfloat16),
            pltpu.VMEM((bag_len, 128, 128), jnp.float32),
        ],
    )
    return pl.pallas_call(
        pool_kernel,
        grid_spec=grid_spec,
        out_shape=jax.ShapeDtypeStruct((blocks * 128, width), jnp.bfloat16),
        compiler_params=pltpu.CompilerParams(
            dimension_semantics=("arbitrary",), vmem_limit_bytes=40 * 1024 * 1024
        ),
    )(order, ids, counts, slots_t, hot_t, own_t)

def merge_pair(stats, axis, size, bit, count):
    mean, m2 = stats[0], stats[1]
    other = lax.ppermute(stats, axis, [(i, i ^ bit) for i in range(size)])
    gap = mean - other[0]
    merged_mean = (mean + other[0]) * 0.5
    merged_m2 = (m2 + other[1]) + gap * gap * (count * 0.5)
    return jnp.stack([merged_mean, merged_m2])


def merge_three(stats, axis, size, stride, count):
    place = lax.axis_index(axis) // stride
    back = lax.ppermute(stats, axis, [(i, (i + stride) % size) for i in range(size)])
    ahead = lax.ppermute(stats, axis, [(i, (i + 2 * stride) % size) for i in range(size)])
    parts = []
    for pos in range(3):
        parts.append(
            jnp.where(place == pos, stats, jnp.where((place + 2) % 3 == pos, back, ahead))
        )
    mean = (parts[0][0] + parts[1][0] + parts[2][0]) / 3.0
    m2 = parts[0][1] + parts[1][1] + parts[2][1]
    spread = (parts[0][0] - mean) ** 2 + (parts[1][0] - mean) ** 2 + (parts[2][0] - mean) ** 2
    return jnp.stack([mean, m2 + spread * count])


def column_stats(values, axes):
    count = float(values.shape[0])
    mean = jnp.sum(values, axis=0) / count
    centered = values - mean
    stats = jnp.stack([mean, jnp.sum(centered * centered, axis=0)])
    for axis, size in axes:
        bit = 1
        while size % (2 * bit) == 0:
            stats = merge_pair(stats, axis, size, bit, count)
            count *= 2
            bit *= 2
        rest = size // bit
        if rest == 3:
            stats = merge_three(stats, axis, size, bit, count)
            count *= 3
        elif rest != 1:
            raise ValueError("axis size")
    return stats[0], stats[1]


def shards(
    table,
    panel_ids,
    bag_slots,
    block_ids,
    bag_counts,
    dense_owner,
    top_weight,
    bn_gain,
    bn_shift,
    out_weight,
):
    row_width = table.shape[1]
    caches = lax.axis_size("cache")
    feat_dev, group_samp, bag_len = bag_slots.shape
    samp_dev = group_samp // caches
    owner_blocks = samp_dev // 128
    group_blocks = group_samp // 128
    blocks_dev = feat_dev * group_blocks
    list_len = block_ids.shape[2]
    cache_ids = jnp.arange(caches, dtype=jnp.int32)
    owner_match = dense_owner[None, :] == cache_ids[:, None]
    inverse = jnp.sum(jnp.where(owner_match, cache_ids[None, :], 0), axis=1)
    block_number = jnp.arange(blocks_dev, dtype=jnp.int32)
    feature_part = block_number // group_blocks
    within_group = block_number % group_blocks
    source_block = (
        feature_part * group_blocks
        + inverse[within_group // owner_blocks] * owner_blocks
        + within_group % owner_blocks
    ).astype(jnp.int32)
    slots_t = jnp.swapaxes(bag_slots.reshape(blocks_dev, 128, bag_len), 1, 2)
    ids = block_ids.reshape(blocks_dev * list_len).astype(jnp.int32)
    counts = bag_counts.reshape(blocks_dev).astype(jnp.int32)
    own_t = table.T
    hot_t = jnp.take(own_t.reshape(row_width, -1, 128), panel_ids, axis=1).reshape(row_width, -1)
    gathered = lax.all_gather(hot_t, "cache", axis=0)
    halves = []
    for half in range(owner_blocks):
        pooled = pool(source_block[half::owner_blocks], ids, counts, slots_t, gathered, own_t)
        pooled = pooled.reshape(feat_dev, caches, 128, row_width)
        features = lax.all_to_all(pooled, "cache", split_axis=1, concat_axis=0, tiled=True)[:, 0]
        products = jnp.einsum("fne,gne->nfg", features, features, preferred_element_type=jnp.float32)
        interaction = (products / math.sqrt(row_width)).astype(jnp.bfloat16)
        flat_rows = interaction.reshape(interaction.shape[0], -1)
        halves.append(jnp.dot(flat_rows, top_weight, preferred_element_type=jnp.float32))
    pre_norm = jnp.concatenate(halves, axis=0)
    col_mean, col_m2 = column_stats(pre_norm, (("cache", caches), ("shard", lax.axis_size("shard"))))
    col_var = col_m2 / (pre_norm.shape[0] * lax.axis_size("shard") * caches)
    normed = (pre_norm - col_mean) * lax.rsqrt(col_var + norm_eps) * bn_gain + bn_shift
    top_hidden = jax.nn.relu(normed).astype(jnp.bfloat16)
    logits = jnp.dot(top_hidden, out_weight, preferred_element_type=jnp.float32)
    return (top_hidden, logits)


def solution(mesh):
    return jax.shard_map(
        shards,
        mesh=mesh,
        in_specs=(
            P(("shard", "cache"), None),
            P(("shard", "cache")),
            P("cache", "shard", None),
            P("cache", "shard", None),
            P("cache", "shard"),
            P("shard"),
            P(),
            P(),
            P(),
            P(),
        ),
        out_specs=(P(("shard", "cache"), None), P(("shard", "cache"))),
        check_vma=False,
    )
```
